1024 devices in a mesh: gx: 16 (over x_hi, y), gy: 16 (over z, core), gz: 4 (over x_lo).
Axes of the slice: x: 8 (x_hi: 2, x_lo: 4; x = x_hi * 4 + x_lo), y: 8, z: 8, core: 2. Of those that a mesh axis runs over, the one named last changes fastest.
Arguments:
- positions: float32 [16, 16, 4, 3, 256], P('gx', 'gy', 'gz'), may hold values from 0.3 to 7.7, as said below
- velocities: float32 [16, 16, 4, 3, 256], P('gx', 'gy', 'gz'), may hold values from -6 to 6
- species: int32 [16, 16, 4, 256], P('gx', 'gy', 'gz'), may hold values from 0 to 3
- pair_table: int32 [16, 16, 4, 3, 1536], P('gx', 'gy', 'gz'), may hold values from 0 to 6911, as said below
- live_blocks: int32 [16, 16, 4], P('gx', 'gy', 'gz'), may hold values from 6 to 12, as said below
- owners: int32 [16, 16, 4, 2], P('gx', 'gy', 'gz'), may hold values from 0 to 3, as said below
- radial_weight: float32 [256, 8], replicated, may hold values from -2 to 2
- center_embed: float32 [256, 4], replicated, may hold values from -3 to 3
- neighbour_embed: float32 [256, 4], replicated, may hold values from -3 to 3
- vector_weight: float32 [32, 8], replicated, may hold values from -2 to 2
- env_weight: float32 [2, 32, 256], replicated, may hold values from -0.375 to 0.375
- vector_gate: float32 [32, 256], replicated, may hold values from -0.375 to 0.375
- latent_weight: float32 [2, 256, 288], replicated, may hold values from -0.375 to 0.375
- energy_weight: float32 [256], replicated, may hold values from -0.375 to 0.375
Outputs:
- migrated: float32 [16, 16, 4, 4, 9, 128], P('gx', 'gy', 'gz')
The draws below stay inside these ranges and needn't reach their ends.
Inputs may be any that keep to these rules, and one draw needn't show every extreme that they name: `positions`: atom k of a domain lies within 0.2 in each coordinate of the point (ix + 0.5, iy + 0.5, iz + 0.5) with k = (8 ix + iy) (4) + iz. `pair_table`: row 0 is a centre atom index below 256; row 1 a neighbour index as in the statement, never the centre itself; row 2 equals the species of that neighbour atom in its own domain. `live_blocks`: some device uses all 12 blocks. The owners of one device's blocks are distinct; in every gz group some device is the owner of one block of every device of the group.
All inputs are finite; a program needn't handle non-finite values.
Results may differ from the reference program's by a relative error of at most 0.0003.
Values sent between devices are 32-bit elements; how exact they have to be, the bound alone decides.
No kernel may reach another device: no remote copies, remote signals or barrier semaphores. Data moves between devices by JAX's collectives and lax.ppermute only.
A program may use at most 32 MiB of HBM per device.

```python
import jax
import jax.numpy as jnp
from jax import lax

LATENT = 256
CHANNELS = 32
RADIAL = 8
SPECIES = 4
LAYERS = 2
BLOCKS = 2
PAIR_BLOCKS = 12
ATOMS_DEV = 256
XDOMAINS = 16
YDOMAINS = 16
ZDOMAINS = 4


def species_common(key):
    return jax.random.randint(jax.random.fold_in(key, 7), (XDOMAINS, YDOMAINS, ZDOMAINS, 128 * BLOCKS), 0, SPECIES)


def draw_species(key, part):
    return species_common(key)


def draw_positions(key, part):
    atoms_here = 128 * BLOCKS
    depth = atoms_here // 64
    labels = jnp.arange(atoms_here)
    lattice = jnp.stack([labels // (8 * depth), labels // depth % 8, labels % depth]).astype(jnp.float32) + 0.5
    shape = (XDOMAINS, YDOMAINS, ZDOMAINS, 3, atoms_here)
    jitter = jnp.clip(0.08 * jax.random.normal(jax.random.fold_in(key, 3), shape, jnp.float32), -0.2, 0.2)
    return lattice + jitter


def draw_pair_table(key, part):
    atoms_here = 128 * BLOCKS
    depth = atoms_here // 64
    pair_count = 128 * PAIR_BLOCKS
    shape = (XDOMAINS, YDOMAINS, ZDOMAINS, pair_count)
    centres = jax.random.randint(jax.random.fold_in(key, 21), shape, 0, atoms_here)
    steps = jax.random.randint(jax.random.fold_in(key, 22), (3,) + shape, -2, 3)
    still = (steps[0] == 0) & (steps[1] == 0) & (steps[2] == 0)
    steps = steps.at[0].set(jnp.where(still, 1, steps[0]))
    cell_x = centres // (8 * depth) + steps[0]
    cell_y = centres // depth % 8 + steps[1]
    cell_z = centres % depth + steps[2]
    hop_x = jnp.floor_divide(cell_x, 8)
    hop_y = jnp.floor_divide(cell_y, 8)
    hop_z = jnp.floor_divide(cell_z, depth)
    local_x = cell_x - hop_x * 8
    local_y = cell_y - hop_y * 8
    local_z = cell_z - hop_z * depth
    slot_index = (hop_x + 1) * 9 + (hop_y + 1) * 3 + (hop_z + 1)
    atom_index = (local_x * 8 + local_y) * depth + local_z
    neighbour = slot_index * atoms_here + atom_index
    grid_x = jnp.arange(XDOMAINS)[:, None, None, None]
    grid_y = jnp.arange(YDOMAINS)[None, :, None, None]
    grid_z = jnp.arange(ZDOMAINS)[None, None, :, None]
    kinds = species_common(key)
    other = kinds[(grid_x + hop_x) % XDOMAINS, (grid_y + hop_y) % YDOMAINS, (grid_z + hop_z) % ZDOMAINS, atom_index]
    return jnp.stack([centres, neighbour, other], axis=3).astype(jnp.int32)


def draw_live_blocks(key, part):
    shape = (XDOMAINS, YDOMAINS, ZDOMAINS)
    counts = jax.random.randint(jax.random.fold_in(key, 31), shape, PAIR_BLOCKS // 2, PAIR_BLOCKS + 1)
    chosen = jax.random.randint(jax.random.fold_in(key, 32), (), 0, XDOMAINS * YDOMAINS * ZDOMAINS)
    flat = counts.reshape(-1)
    flat = jnp.where(jnp.arange(flat.shape[0]) == chosen, PAIR_BLOCKS, flat)
    return flat.reshape(shape).astype(jnp.int32)


def draw_owners(key, part):
    shape = (XDOMAINS, YDOMAINS, ZDOMAINS)
    receiver = jax.random.randint(jax.random.fold_in(key, 41), (XDOMAINS, YDOMAINS, 1), 0, ZDOMAINS)
    receiver = jnp.broadcast_to(receiver, shape)
    scores = jax.random.randint(jax.random.fold_in(key, 42), shape + (ZDOMAINS,), 0, 1 << 20) * ZDOMAINS + jnp.arange(ZDOMAINS)
    scores = jnp.where(jnp.arange(ZDOMAINS) == receiver[..., None], -1, scores)
    order = jnp.argsort(scores, axis=-1, stable=True)
    turn = jax.random.randint(jax.random.fold_in(key, 43), shape + (1,), 0, BLOCKS)
    picks = (jnp.arange(BLOCKS) + turn) % BLOCKS
    return jnp.take_along_axis(order, picks, axis=-1).astype(jnp.int32)


def levels(key, dims, pieces, smallest, top_value):
    def one(axis_at, blocks):
        draws = jax.random.uniform(jax.random.fold_in(jax.random.fold_in(key, 6), axis_at), (blocks,), jnp.float32, smallest / len(pieces), top_value / len(pieces))
        return jnp.repeat(jnp.exp(draws), dims[axis_at] // blocks).reshape((-1,) + (1,) * (len(dims) - axis_at - 1))

    level = one(*pieces[0])
    for cut in pieces[1:]:
        level = level * one(*cut)
    return level


def bell_draw(key, extent, width, bound, shards=(), kind=jnp.bfloat16):
    entries = width * jax.random.normal(key, extent, jnp.float32)
    if shards:
        entries = entries * levels(key, extent, shards, -0.22, 0.18)
    return jnp.clip(entries, -bound, bound).astype(kind)


def setup_inputs(seed: int = 0) -> dict:
    seeds = jax.random.split(jax.random.key(seed), 15)
    return {
        "positions": draw_positions(jax.random.fold_in(seeds[14], 71), 0),
        "velocities": bell_draw(seeds[1], (XDOMAINS, YDOMAINS, ZDOMAINS, 3, ATOMS_DEV), 1.0, 6.0, ((0, 16), (1, 16), (2, 4)), jnp.float32),
        "species": draw_species(jax.random.fold_in(seeds[14], 71), 0),
        "pair_table": draw_pair_table(jax.random.fold_in(seeds[14], 71), 0),
        "live_blocks": draw_live_blocks(jax.random.fold_in(seeds[14], 71), 0),
        "owners": draw_owners(jax.random.fold_in(seeds[14], 71), 0),
        "radial_weight": bell_draw(seeds[6], (LATENT, RADIAL), RADIAL ** -0.5, 2.0, (), jnp.float32),
        "center_embed": bell_draw(seeds[7], (LATENT, SPECIES), SPECIES ** -0.5, 3.0, (), jnp.float32),
        "neighbour_embed": bell_draw(seeds[8], (LATENT, SPECIES), SPECIES ** -0.5, 3.0, (), jnp.float32),
        "vector_weight": bell_draw(seeds[9], (CHANNELS, RADIAL), RADIAL ** -0.5, 2.0, (), jnp.float32),
        "env_weight": bell_draw(seeds[10], (LAYERS, CHANNELS, LATENT), LATENT ** -0.5, 0.375, (), jnp.float32),
        "vector_gate": bell_draw(seeds[11], (CHANNELS, LATENT), LATENT ** -0.5, 0.375, (), jnp.float32),
        "latent_weight": bell_draw(seeds[12], (LAYERS, LATENT, LATENT + CHANNELS), (LATENT + CHANNELS) ** -0.5, 0.375, (), jnp.float32),
        "energy_weight": bell_draw(seeds[13], (LATENT,), LATENT ** -0.5, 0.375, (), jnp.float32),
    }


CUTOFF = 5.0
ENV_SCALE = 0.4
TIME_STEP = 0.2

def matmul(left, right):
    return jnp.dot(left, right, precision=lax.Precision.HIGHEST)

def pair_energy(extended, pair_rows, live_count, own_species, radial_weight, center_embed, neighbour_embed, vector_weight, env_weight, vector_gate, latent_weight, energy_weight):
    atoms_here = own_species.shape[0]
    pair_count = pair_rows.shape[1]
    depth = atoms_here // 64
    centres = pair_rows[0]
    neighbour = pair_rows[1]
    other_species = pair_rows[2]
    slot_index = neighbour // atoms_here
    atom_index = neighbour - slot_index * atoms_here
    offset_x = (slot_index // 9 - 1).astype(jnp.float32) * 8.0
    offset_y = (slot_index // 3 % 3 - 1).astype(jnp.float32) * 8.0
    offset_z = (slot_index % 3 - 1).astype(jnp.float32) * float(depth)
    shifts = jnp.stack([offset_x, offset_y, offset_z])
    far_end = extended[slot_index, :, atom_index].T
    near_end = extended[13, :, centres].T
    displace = far_end + shifts - near_end
    distance = jnp.sqrt(lax.optimization_barrier(jnp.sum(displace * displace, axis=0)))
    unit = displace / distance
    orders = jnp.arange(1, radial_weight.shape[1] + 1).astype(jnp.float32)
    basis = jnp.sqrt(2.0 / CUTOFF) * jnp.sin(orders[:, None] * jnp.pi * distance[None] / CUTOFF) / distance[None]
    ratio = distance / CUTOFF
    in_use = (jnp.arange(pair_count) < live_count * 128).astype(jnp.float32)
    envelope = (1.0 - ratio * ratio) ** 2 * in_use
    kinds = jnp.arange(center_embed.shape[1])[:, None]
    centre_hot = (kinds == own_species[centres][None]).astype(jnp.float32)
    other_hot = (kinds == other_species[None]).astype(jnp.float32)
    latent = envelope[None] * jax.nn.silu(matmul(radial_weight, basis) + matmul(center_embed, centre_hot) + matmul(neighbour_embed, other_hot))
    channels = vector_weight.shape[0]
    vectors = envelope[None, None] * matmul(vector_weight, basis)[None] * unit[:, None, :]
    member = (centres[:, None] == jnp.arange(atoms_here)[None]).astype(jnp.float32)
    n_layers = env_weight.shape[0]
    for layer in range(n_layers):
        env_pairs = matmul(env_weight[layer], latent)
        spread = (unit[:, None, :] * env_pairs[None]).reshape(3 * channels, pair_count)
        environment = ENV_SCALE * matmul(spread, member)
        at_pairs = lax.dot_general(environment, member, (((1,), (1,)), ((), ())), precision=lax.Precision.HIGHEST)
        at_pairs = at_pairs.reshape(3, channels, pair_count)
        scalars = lax.optimization_barrier(jnp.sum(vectors * at_pairs, axis=0))
        update = matmul(latent_weight[layer], jnp.concatenate([latent, scalars], axis=0))
        if layer + 1 < n_layers:
            vectors = vectors + at_pairs * matmul(vector_gate, latent)[None]
        latent = latent + envelope[None] * jax.nn.silu(update)
    return jnp.sum(matmul(energy_weight[None], latent))

def reference(positions, velocities, species, pair_table, live_blocks, owners, radial_weight, center_embed, neighbour_embed, vector_weight, env_weight, vector_gate, latent_weight, energy_weight):
    xcount, ycount, zcount, _, atoms_here = positions.shape
    depth = atoms_here // 64
    padded = jnp.pad(positions, ((1, 1), (1, 1), (1, 1), (0, 0), (0, 0)), mode='wrap')

    def one_domain(flat):
        grid_x = flat // (ycount * zcount)
        grid_y = flat // zcount % ycount
        grid_z = flat % zcount
        zero = grid_x * 0
        block = lax.dynamic_slice(padded, (grid_x, grid_y, grid_z, zero, zero), (3, 3, 3, 3, atoms_here))
        extended = block.reshape(27, 3, atoms_here)
        grad = jax.grad(pair_energy)(extended, pair_table[grid_x, grid_y, grid_z], live_blocks[grid_x, grid_y, grid_z], species[grid_x, grid_y, grid_z], radial_weight, center_embed, neighbour_embed, vector_weight, env_weight, vector_gate, latent_weight, energy_weight)
        return grad.reshape(3, 3, 3, 3, atoms_here)
    grads = lax.map(one_domain, jnp.arange(xcount * ycount * zcount, dtype=jnp.int32))
    grads = grads.reshape(xcount, ycount, zcount, 3, 3, 3, 3, atoms_here)
    forces = jnp.zeros((xcount, ycount, zcount, 3, atoms_here), jnp.float32)
    for step_x in range(3):
        for step_y in range(3):
            for step_z in range(3):
                forces = forces - jnp.roll(grads[:, :, :, step_x, step_y, step_z], (step_x - 1, step_y - 1, step_z - 1), axis=(0, 1, 2))
    inverse_mass = 1.0 / (1.0 + species.astype(jnp.float32))
    new_vel = velocities + TIME_STEP * forces * inverse_mass[:, :, :, None, :]
    new_pos = positions + TIME_STEP * new_vel
    state = jnp.concatenate([new_pos, new_vel, forces], axis=3)
    blocks_count = atoms_here // 128
    blocks = state.reshape(xcount, ycount, zcount, 9, blocks_count, 128).transpose(0, 1, 2, 4, 3, 5)
    hits = (owners[..., None] == jnp.arange(zcount)).astype(jnp.float32)
    moved = jnp.einsum('xysbd,xysbcq->xydscq', hits, blocks, precision=lax.Precision.HIGHEST)
    flags = lax.optimization_barrier(jnp.sum(hits, axis=3)).transpose(0, 1, 3, 2)
    source = jnp.arange(zcount)[None, None, None, :]
    target = jnp.arange(zcount)[None, None, :, None]
    rise = flags * (source - target).astype(jnp.float32) * float(depth)
    moved = moved.at[:, :, :, :, 2, :].add(rise[..., None])
    return moved
```

```python
import jax
import jax.numpy as jnp
from jax import lax
from jax.sharding import PartitionSpec as P

CUTOFF = 5.0
ENV_SCALE = 0.4
TIME_STEP = 0.2


def ring_pairs(axis):
    count = lax.axis_size(axis)
    forward = [(i, (i + 1) % count) for i in range(count)]
    backward = [(target, source) for source, target in forward]
    return forward, backward


def extended_2(block, sides, width):
    for axis, dim in sides:
        forward, backward = ring_pairs(axis)
        low = lax.ppermute(
            lax.slice_in_dim(block, block.shape[dim] - width, None, axis=dim), axis, forward
        )
        high = lax.ppermute(lax.slice_in_dim(block, 0, width, axis=dim), axis, backward)
        block = jnp.concatenate([low, block, high], axis=dim)
    return block


def fold_halo(grad, axes):
    for axis in axes:
        forward, backward = ring_pairs(axis)
        from_low = lax.ppermute(grad[2], axis, forward)
        from_high = lax.ppermute(grad[0], axis, backward)
        grad = grad[1] + from_low + from_high
    return grad


def matmul(left, right):
    return jnp.dot(left, right, precision=lax.Precision.HIGHEST)


def matmul_t(left, right):
    return lax.dot_general(
        left, right, (((1,), (1,)), ((), ())), precision=lax.Precision.HIGHEST
    )


def pair_energy(
    extended,
    pair_rows,
    live_count,
    own_species,
    radial_weight,
    center_embed,
    neighbour_embed,
    vector_weight,
    env_weight,
    vector_gate,
    latent_weight,
    energy_weight,
):
    slots, _, atoms_here = extended.shape
    pair_count = pair_rows.shape[1]
    depth = atoms_here // 64
    centres = pair_rows[0]
    neighbour = pair_rows[1]
    other_species = pair_rows[2]
    slot_index = neighbour // atoms_here
    atom_index = neighbour - slot_index * atoms_here
    offset_x = (slot_index // 9 - 1).astype(jnp.float32) * 8.0
    offset_y = (slot_index // 3 % 3 - 1).astype(jnp.float32) * 8.0
    offset_z = (slot_index % 3 - 1).astype(jnp.float32) * float(depth)
    shifts = jnp.stack([offset_x, offset_y, offset_z])
    atoms = jnp.arange(atoms_here)
    atom_hot = (atoms[:, None] == atom_index[None]).astype(jnp.float32)
    slot_hot = (jnp.arange(slots)[:, None] == slot_index[None]).astype(jnp.float32)
    member = (centres[:, None] == atoms[None]).astype(jnp.float32)
    by_atom = matmul(extended.reshape(slots * 3, atoms_here), atom_hot)
    far_end = jnp.sum(by_atom.reshape(slots, 3, pair_count) * slot_hot[:, None, :], axis=0)
    near_end = matmul_t(extended[13], member)
    displace = far_end + shifts - near_end
    distance = jnp.sqrt(jnp.sum(displace * displace, axis=0))
    unit = displace / distance
    orders = jnp.arange(1, radial_weight.shape[1] + 1).astype(jnp.float32)
    basis = (
        jnp.sqrt(2.0 / CUTOFF)
        * jnp.sin(orders[:, None] * jnp.pi * distance[None] / CUTOFF)
        / distance[None]
    )
    ratio = distance / CUTOFF
    in_use = (jnp.arange(pair_count) < live_count * 128).astype(jnp.float32)
    envelope = (1.0 - ratio * ratio) ** 2 * in_use
    kinds = jnp.arange(center_embed.shape[1])[:, None]
    species_hot = (kinds == own_species[None]).astype(jnp.float32)
    centre_hot = matmul_t(species_hot, member)
    other_hot = (kinds == other_species[None]).astype(jnp.float32)
    latent = envelope[None] * jax.nn.silu(
        matmul(radial_weight, basis)
        + matmul(center_embed, centre_hot)
        + matmul(neighbour_embed, other_hot)
    )
    channels = vector_weight.shape[0]
    vectors = envelope[None, None] * matmul(vector_weight, basis)[None] * unit[:, None, :]
    n_layers = env_weight.shape[0]
    for layer in range(n_layers):
        env_pairs = matmul(env_weight[layer], latent)
        spread = (unit[:, None, :] * env_pairs[None]).reshape(3 * channels, pair_count)
        environment = ENV_SCALE * matmul(spread, member)
        at_pairs = matmul_t(environment, member)
        at_pairs = at_pairs.reshape(3, channels, pair_count)
        scalars = jnp.sum(vectors * at_pairs, axis=0)
        update = matmul(latent_weight[layer], jnp.concatenate([latent, scalars], axis=0))
        if layer + 1 < n_layers:
            vectors = vectors + at_pairs * matmul(vector_gate, latent)[None]
        latent = latent + envelope[None] * jax.nn.silu(update)
    return jnp.sum(matmul(energy_weight[None], latent))


def per_device(
    positions,
    velocities,
    species,
    pair_table,
    live_blocks,
    owners,
    radial_weight,
    center_embed,
    neighbour_embed,
    vector_weight,
    env_weight,
    vector_gate,
    latent_weight,
    energy_weight,
):
    atoms_here = positions.shape[4]
    depth = atoms_here // 64
    zcount = lax.axis_size("gz")
    beside_all = extended_2(positions, (("gx", 0), ("gy", 1), ("gz", 2)), 1)
    extended = beside_all.reshape(27, 3, atoms_here)
    own_species = species[0, 0, 0]
    grad = jax.grad(pair_energy)(
        extended,
        pair_table[0, 0, 0],
        live_blocks[0, 0, 0],
        own_species,
        radial_weight,
        center_embed,
        neighbour_embed,
        vector_weight,
        env_weight,
        vector_gate,
        latent_weight,
        energy_weight,
    )
    grad = grad.reshape(3, 3, 3, 3, atoms_here)
    forces = -fold_halo(grad, ("gx", "gy", "gz"))
    inverse_mass = 1.0 / (1.0 + own_species.astype(jnp.float32))
    new_vel = velocities[0, 0, 0] + TIME_STEP * forces * inverse_mass[None]
    new_pos = positions[0, 0, 0] + TIME_STEP * new_vel
    state = jnp.concatenate([new_pos, new_vel, forces], axis=0)
    blocks_count = atoms_here // 128
    blocks = state.reshape(9, blocks_count, 128).transpose(1, 0, 2)
    hits = (owners[0, 0, 0][:, None] == jnp.arange(zcount)[None]).astype(jnp.float32)
    outgoing = jnp.einsum("bd,bcq->dcq", hits, blocks, precision=lax.Precision.HIGHEST)
    sent = jnp.sum(hits, axis=0)
    myself = lax.axis_index("gz")
    target = jnp.arange(zcount, dtype=jnp.int32)
    rise = sent * (myself - target).astype(jnp.float32) * float(depth)
    outgoing = outgoing.at[:, 2, :].add(rise[:, None])
    arrived = lax.all_to_all(outgoing, "gz", split_axis=0, concat_axis=0, tiled=True)
    return arrived[None, None, None]


def solution(mesh):
    in_specs = (
        P("gx", "gy", "gz", None, None),
        P("gx", "gy", "gz", None, None),
        P("gx", "gy", "gz", None),
        P("gx", "gy", "gz", None, None),
        P("gx", "gy", "gz"),
        P("gx", "gy", "gz", None),
        P(),
        P(),
        P(),
        P(),
        P(),
        P(),
        P(),
        P(),
    )
    out_specs = P("gx", "gy", "gz", None, None, None)
    return jax.shard_map(
        per_device, mesh=mesh, in_specs=in_specs, out_specs=out_specs, check_vma=False
    )
```

```python
import jax
import jax.numpy as jnp
from jax import lax
from jax.sharding import PartitionSpec as P

CUTOFF = 5.0
ENV_SCALE = 0.4
TIME_STEP = 0.2


def ring_pairs(axis):
    count = lax.axis_size(axis)
    forward = [(i, (i + 1) % count) for i in range(count)]
    backward = [(target, source) for source, target in forward]
    return forward, backward


def extended_2(block, sides, width):
    for axis, dim in sides:
        forward, backward = ring_pairs(axis)
        low = lax.ppermute(
            lax.slice_in_dim(block, block.shape[dim] - width, None, axis=dim), axis, forward
        )
        high = lax.ppermute(lax.slice_in_dim(block, 0, width, axis=dim), axis, backward)
        block = jnp.concatenate([low, block, high], axis=dim)
    return block


def fold_halo(grad, axes):
    for axis in axes:
        forward, backward = ring_pairs(axis)
        from_low = lax.ppermute(grad[2], axis, forward)
        from_high = lax.ppermute(grad[0], axis, backward)
        grad = grad[1] + from_low + from_high
    return grad


def matmul(left, right, precision=lax.Precision.HIGH):
    return jnp.dot(left, right, precision=precision)


def matmul_t(left, right, precision=lax.Precision.HIGH):
    return lax.dot_general(left, right, (((1,), (1,)), ((), ())), precision=precision)


def pair_energy(
    extended,
    pair_rows,
    live_count,
    own_species,
    radial_weight,
    center_embed,
    neighbour_embed,
    vector_weight,
    env_weight,
    vector_gate,
    latent_weight,
    energy_weight,
):
    slots, _, atoms_here = extended.shape
    pair_count = pair_rows.shape[1]
    depth = atoms_here // 64
    centres = pair_rows[0]
    neighbour = pair_rows[1]
    other_species = pair_rows[2]
    slot_index = neighbour // atoms_here
    atom_index = neighbour - slot_index * atoms_here
    offset_x = (slot_index // 9 - 1).astype(jnp.float32) * 8.0
    offset_y = (slot_index // 3 % 3 - 1).astype(jnp.float32) * 8.0
    offset_z = (slot_index % 3 - 1).astype(jnp.float32) * float(depth)
    shifts = jnp.stack([offset_x, offset_y, offset_z])
    atoms = jnp.arange(atoms_here)
    atom_hot = (atoms[:, None] == atom_index[None]).astype(jnp.float32)
    slot_hot = (jnp.arange(slots)[:, None] == slot_index[None]).astype(jnp.float32)
    member = (centres[:, None] == atoms[None]).astype(jnp.float32)
    by_atom = matmul(
        extended.reshape(slots * 3, atoms_here), atom_hot, lax.Precision.HIGHEST
    )
    far_end = jnp.sum(by_atom.reshape(slots, 3, pair_count) * slot_hot[:, None, :], axis=0)
    near_end = matmul_t(extended[13], member, lax.Precision.HIGHEST)
    displace = far_end + shifts - near_end
    distance = jnp.sqrt(jnp.sum(displace * displace, axis=0))
    unit = displace / distance
    orders = jnp.arange(1, radial_weight.shape[1] + 1).astype(jnp.float32)
    basis = (
        jnp.sqrt(2.0 / CUTOFF)
        * jnp.sin(orders[:, None] * jnp.pi * distance[None] / CUTOFF)
        / distance[None]
    )
    ratio = distance / CUTOFF
    in_use = (jnp.arange(pair_count) < live_count * 128).astype(jnp.float32)
    envelope = (1.0 - ratio * ratio) ** 2 * in_use
    kinds = jnp.arange(center_embed.shape[1])[:, None]
    species_hot = (kinds == own_species[None]).astype(jnp.float32)
    centre_hot = matmul_t(species_hot, member)
    other_hot = (kinds == other_species[None]).astype(jnp.float32)
    latent = envelope[None] * jax.nn.silu(
        matmul(radial_weight, basis)
        + matmul(center_embed, centre_hot)
        + matmul(neighbour_embed, other_hot)
    )
    channels = vector_weight.shape[0]
    vectors = envelope[None, None] * matmul(vector_weight, basis)[None] * unit[:, None, :]
    n_layers = env_weight.shape[0]
    for layer in range(n_layers):
        env_pairs = matmul(env_weight[layer], latent)
        spread = (unit[:, None, :] * env_pairs[None]).reshape(3 * channels, pair_count)
        environment = ENV_SCALE * matmul(spread, member)
        at_pairs = matmul_t(environment, member)
        at_pairs = at_pairs.reshape(3, channels, pair_count)
        scalars = jnp.sum(vectors * at_pairs, axis=0)
        update = matmul(latent_weight[layer], jnp.concatenate([latent, scalars], axis=0))
        if layer + 1 < n_layers:
            vectors = vectors + at_pairs * matmul(vector_gate, latent)[None]
        latent = latent + envelope[None] * jax.nn.silu(update)
    return jnp.sum(matmul(energy_weight[None], latent))


def per_device(
    positions,
    velocities,
    species,
    pair_table,
    live_blocks,
    owners,
    radial_weight,
    center_embed,
    neighbour_embed,
    vector_weight,
    env_weight,
    vector_gate,
    latent_weight,
    energy_weight,
):
    atoms_here = positions.shape[4]
    depth = atoms_here // 64
    zcount = lax.axis_size("gz")
    beside_all = extended_2(positions, (("gx", 0), ("gy", 1), ("gz", 2)), 1)
    extended = beside_all.reshape(27, 3, atoms_here)
    own_species = species[0, 0, 0]
    grad = jax.grad(pair_energy)(
        extended,
        pair_table[0, 0, 0],
        live_blocks[0, 0, 0],
        own_species,
        radial_weight,
        center_embed,
        neighbour_embed,
        vector_weight,
        env_weight,
        vector_gate,
        latent_weight,
        energy_weight,
    )
    grad = grad.reshape(3, 3, 3, 3, atoms_here)
    forces = -fold_halo(grad, ("gx", "gy", "gz"))
    inverse_mass = 1.0 / (1.0 + own_species.astype(jnp.float32))
    new_vel = velocities[0, 0, 0] + TIME_STEP * forces * inverse_mass[None]
    new_pos = positions[0, 0, 0] + TIME_STEP * new_vel
    state = jnp.concatenate([new_pos, new_vel, forces], axis=0)
    blocks_count = atoms_here // 128
    blocks = state.reshape(9, blocks_count, 128).transpose(1, 0, 2)
    hits = (owners[0, 0, 0][:, None] == jnp.arange(zcount)[None]).astype(jnp.float32)
    outgoing = jnp.einsum("bd,bcq->dcq", hits, blocks, precision=lax.Precision.HIGHEST)
    sent = jnp.sum(hits, axis=0)
    myself = lax.axis_index("gz")
    target = jnp.arange(zcount, dtype=jnp.int32)
    rise = sent * (myself - target).astype(jnp.float32) * float(depth)
    outgoing = outgoing.at[:, 2, :].add(rise[:, None])
    arrived = lax.all_to_all(outgoing, "gz", split_axis=0, concat_axis=0, tiled=True)
    return arrived[None, None, None]


def solution(mesh):
    in_specs = (
        P("gx", "gy", "gz", None, None),
        P("gx", "gy", "gz", None, None),
        P("gx", "gy", "gz", None),
        P("gx", "gy", "gz", None, None),
        P("gx", "gy", "gz"),
        P("gx", "gy", "gz", None),
        P(),
        P(),
        P(),
        P(),
        P(),
        P(),
        P(),
        P(),
    )
    out_specs = P("gx", "gy", "gz", None, None, None)
    return jax.shard_map(
        per_device, mesh=mesh, in_specs=in_specs, out_specs=out_specs, check_vma=False
    )
```

```python
import jax
import jax.numpy as jnp
from jax import lax
from jax.sharding import PartitionSpec as P

CUTOFF = 5.0
ENV_SCALE = 0.4
TIME_STEP = 0.2


def ring_pairs(axis):
    count = lax.axis_size(axis)
    forward = [(i, (i + 1) % count) for i in range(count)]
    backward = [(target, source) for source, target in forward]
    return forward, backward


def extended_2(block, sides, width):
    for axis, dim in sides:
        forward, backward = ring_pairs(axis)
        low = lax.ppermute(
            lax.slice_in_dim(block, block.shape[dim] - width, None, axis=dim), axis, forward
        )
        high = lax.ppermute(lax.slice_in_dim(block, 0, width, axis=dim), axis, backward)
        block = jnp.concatenate([low, block, high], axis=dim)
    return block


def fold_halo(grad, axes):
    for axis in axes:
        forward, backward = ring_pairs(axis)
        from_low = lax.ppermute(grad[2], axis, forward)
        from_high = lax.ppermute(grad[0], axis, backward)
        grad = grad[1] + from_low + from_high
    return grad


def matmul(left, right, precision=lax.Precision.HIGH):
    return jnp.dot(left, right, precision=precision)


def matmul_t(left, right, precision=lax.Precision.HIGH):
    return lax.dot_general(left, right, (((1,), (1,)), ((), ())), precision=precision)


def pair_energy(
    extended,
    pair_rows,
    live_count,
    own_species,
    radial_weight,
    center_embed,
    neighbour_embed,
    vector_weight,
    env_weight,
    vector_gate,
    latent_weight,
    energy_weight,
):
    slots, _, atoms_here = extended.shape
    pair_count = pair_rows.shape[1]
    depth = atoms_here // 64
    centres = pair_rows[0]
    neighbour = pair_rows[1]
    other_species = pair_rows[2]
    slot_index = neighbour // atoms_here
    atom_index = neighbour - slot_index * atoms_here
    offset_x = (slot_index // 9 - 1).astype(jnp.float32) * 8.0
    offset_y = (slot_index // 3 % 3 - 1).astype(jnp.float32) * 8.0
    offset_z = (slot_index % 3 - 1).astype(jnp.float32) * float(depth)
    shifts = jnp.stack([offset_x, offset_y, offset_z])
    atoms = jnp.arange(atoms_here)
    atom_hot = (atoms[:, None] == atom_index[None]).astype(jnp.float32)
    slot_hot = (jnp.arange(slots)[:, None] == slot_index[None]).astype(jnp.float32)
    member = (centres[:, None] == atoms[None]).astype(jnp.float32)
    by_atom = matmul(
        extended.reshape(slots * 3, atoms_here), atom_hot, lax.Precision.HIGHEST
    )
    far_end = jnp.sum(by_atom.reshape(slots, 3, pair_count) * slot_hot[:, None, :], axis=0)
    near_end = matmul_t(extended[13], member, lax.Precision.HIGHEST)
    displace = far_end + shifts - near_end
    distance = jnp.sqrt(jnp.sum(displace * displace, axis=0))
    unit = displace / distance
    orders = jnp.arange(1, radial_weight.shape[1] + 1).astype(jnp.float32)
    basis = (
        jnp.sqrt(2.0 / CUTOFF)
        * jnp.sin(orders[:, None] * jnp.pi * distance[None] / CUTOFF)
        / distance[None]
    )
    ratio = distance / CUTOFF
    in_use = (jnp.arange(pair_count) < live_count * 128).astype(jnp.float32)
    envelope = (1.0 - ratio * ratio) ** 2 * in_use
    kinds = jnp.arange(center_embed.shape[1])[:, None]
    species_hot = (kinds == own_species[None]).astype(jnp.float32)
    centre_hot = matmul_t(species_hot, member)
    other_hot = (kinds == other_species[None]).astype(jnp.float32)
    latent = envelope[None] * jax.nn.silu(
        matmul(radial_weight, basis)
        + matmul(center_embed, centre_hot)
        + matmul(neighbour_embed, other_hot)
    )
    channels = vector_weight.shape[0]
    vectors = envelope[None, None] * matmul(vector_weight, basis)[None] * unit[:, None, :]
    n_layers = env_weight.shape[0]
    for layer in range(n_layers):
        env_pairs = matmul(env_weight[layer], latent)
        spread = (unit[:, None, :] * env_pairs[None]).reshape(3 * channels, pair_count)
        environment = ENV_SCALE * matmul(spread, member)
        at_pairs = matmul_t(environment, member)
        at_pairs = at_pairs.reshape(3, channels, pair_count)
        scalars = jnp.sum(vectors * at_pairs, axis=0)
        update = matmul(latent_weight[layer], jnp.concatenate([latent, scalars], axis=0))
        if layer + 1 < n_layers:
            vectors = vectors + at_pairs * matmul(vector_gate, latent)[None]
        latent = latent + envelope[None] * jax.nn.silu(update)
    return jnp.sum(matmul(energy_weight[None], latent))


def per_device(
    positions,
    velocities,
    species,
    pair_table,
    live_blocks,
    owners,
    radial_weight,
    center_embed,
    neighbour_embed,
    vector_weight,
    env_weight,
    vector_gate,
    latent_weight,
    energy_weight,
):
    atoms_here = positions.shape[4]
    depth = atoms_here // 64
    zcount = lax.axis_size("gz")
    blocks_count = atoms_here // 128
    own_owners = owners[0, 0, 0]
    owner_row = jnp.repeat(own_owners.astype(jnp.float32), 128)
    carried = jnp.concatenate([positions, owner_row.reshape(1, 1, 1, 1, atoms_here)], axis=3)
    beside_all = extended_2(carried, (("gx", 0), ("gy", 1), ("gz", 2)), 1)
    extended = beside_all[:, :, :, :3].reshape(27, 3, atoms_here)
    beside_owners = beside_all[1, 1, :, 3]
    own_species = species[0, 0, 0]
    grad = jax.grad(pair_energy)(
        extended,
        pair_table[0, 0, 0],
        live_blocks[0, 0, 0],
        own_species,
        radial_weight,
        center_embed,
        neighbour_embed,
        vector_weight,
        env_weight,
        vector_gate,
        latent_weight,
        energy_weight,
    )
    grad = grad.reshape(3, 3, 3, 3, atoms_here)
    partial = fold_halo(grad, ("gx", "gy"))
    myself = lax.axis_index("gz")
    receivers = jnp.arange(zcount)
    sources = jnp.arange(zcount)
    beside_hits = (
        beside_owners.reshape(3, blocks_count, 128)[:, :, 0, None] == receivers.astype(jnp.float32)
    ).astype(jnp.float32)
    partial_blocks = partial.reshape(3, 3, blocks_count, 128).transpose(0, 2, 1, 3)
    per_receiver = jnp.sum(beside_hits[:, :, :, None, None] * partial_blocks[:, :, None], axis=1)
    source_of = (sources[None] == (myself + jnp.arange(3)[:, None] - 1) % zcount).astype(jnp.float32)
    grad_out = jnp.sum(source_of[:, None, :, None, None] * per_receiver[:, :, None], axis=0)
    inverse_mass = 1.0 / (1.0 + own_species.astype(jnp.float32))
    own_rows = jnp.concatenate(
        [positions[0, 0, 0], velocities[0, 0, 0], inverse_mass[None], jnp.ones((1, atoms_here), jnp.float32)],
        axis=0,
    )
    own_blocks = own_rows.reshape(8, blocks_count, 128).transpose(1, 0, 2)
    hits = (own_owners[:, None] == receivers[None]).astype(jnp.float32)
    own_out = jnp.sum(hits[:, :, None, None] * own_blocks[:, None], axis=0)
    at_self = (sources == myself).astype(jnp.float32)
    own_out = at_self[None, :, None, None] * own_out[:, None]
    outgoing = jnp.concatenate([grad_out, own_out], axis=2)
    arrived = lax.all_to_all(outgoing, "gz", split_axis=0, concat_axis=0, tiled=True)
    gathered = jnp.sum(arrived, axis=0)
    forces = -gathered[:, 0:3]
    old_pos = gathered[:, 3:6]
    old_vel = gathered[:, 6:9]
    arrived_mass = gathered[:, 9:10]
    flags = gathered[:, 10, 0]
    new_vel = old_vel + TIME_STEP * forces * arrived_mass
    new_pos = old_pos + TIME_STEP * new_vel
    state = jnp.concatenate([new_pos, new_vel, forces], axis=1)
    rise = flags * (sources - myself).astype(jnp.float32) * float(depth)
    arrived = state.at[:, 2, :].add(rise[:, None])
    return arrived[None, None, None]


def solution(mesh):
    in_specs = (
        P("gx", "gy", "gz", None, None),
        P("gx", "gy", "gz", None, None),
        P("gx", "gy", "gz", None),
        P("gx", "gy", "gz", None, None),
        P("gx", "gy", "gz"),
        P("gx", "gy", "gz", None),
        P(),
        P(),
        P(),
        P(),
        P(),
        P(),
        P(),
        P(),
    )
    out_specs = P("gx", "gy", "gz", None, None, None)
    return jax.shard_map(
        per_device, mesh=mesh, in_specs=in_specs, out_specs=out_specs, check_vma=False
    )
```

```python
import jax
import jax.numpy as jnp
from jax import lax
from jax.sharding import PartitionSpec as P

CUTOFF = 5.0
ENV_SCALE = 0.4
TIME_STEP = 0.2


def ring_pairs(axis):
    count = lax.axis_size(axis)
    forward = [(i, (i + 1) % count) for i in range(count)]
    backward = [(target, source) for source, target in forward]
    return forward, backward


def extended_2(block, sides, width):
    for axis, dim in sides:
        forward, backward = ring_pairs(axis)
        low = lax.ppermute(
            lax.slice_in_dim(block, block.shape[dim] - width, None, axis=dim), axis, forward
        )
        high = lax.ppermute(lax.slice_in_dim(block, 0, width, axis=dim), axis, backward)
        block = jnp.concatenate([low, block, high], axis=dim)
    return block


def fold_halo(grad, axes):
    for axis in axes:
        forward, backward = ring_pairs(axis)
        from_low = lax.ppermute(grad[2], axis, forward)
        from_high = lax.ppermute(grad[0], axis, backward)
        grad = grad[1] + from_low + from_high
    return grad


def matmul(left, right, precision=lax.Precision.HIGH):
    return jnp.dot(left, right, precision=precision)


def matmul_t(left, right, precision=lax.Precision.HIGH):
    return lax.dot_general(left, right, (((1,), (1,)), ((), ())), precision=precision)


def pair_energy(
    extended,
    pair_rows,
    live_count,
    own_species,
    radial_weight,
    center_embed,
    neighbour_embed,
    vector_weight,
    env_weight,
    vector_gate,
    latent_weight,
    energy_weight,
):
    slots, _, atoms_here = extended.shape
    pair_count = pair_rows.shape[1]
    depth = atoms_here // 64
    centres = pair_rows[0]
    neighbour = pair_rows[1]
    other_species = pair_rows[2]
    slot_index = neighbour // atoms_here
    atom_index = neighbour - slot_index * atoms_here
    offset_x = (slot_index // 9 - 1).astype(jnp.float32) * 8.0
    offset_y = (slot_index // 3 % 3 - 1).astype(jnp.float32) * 8.0
    offset_z = (slot_index % 3 - 1).astype(jnp.float32) * float(depth)
    shifts = jnp.stack([offset_x, offset_y, offset_z])
    atoms = jnp.arange(atoms_here)
    atom_hot = (atoms[:, None] == atom_index[None]).astype(jnp.float32)
    slot_hot = (jnp.arange(slots)[:, None] == slot_index[None]).astype(jnp.float32)
    member = (centres[:, None] == atoms[None]).astype(jnp.float32)
    by_atom = matmul(
        extended.reshape(slots * 3, atoms_here), atom_hot, lax.Precision.HIGHEST
    )
    far_end = jnp.sum(by_atom.reshape(slots, 3, pair_count) * slot_hot[:, None, :], axis=0)
    near_end = matmul_t(extended[13], member, lax.Precision.HIGHEST)
    displace = far_end + shifts - near_end
    distance = jnp.sqrt(jnp.sum(displace * displace, axis=0))
    unit = displace / distance
    orders = jnp.arange(1, radial_weight.shape[1] + 1).astype(jnp.float32)
    basis = (
        jnp.sqrt(2.0 / CUTOFF)
        * jnp.sin(orders[:, None] * jnp.pi * distance[None] / CUTOFF)
        / distance[None]
    )
    ratio = distance / CUTOFF
    in_use = (jnp.arange(pair_count) < live_count * 128).astype(jnp.float32)
    envelope = (1.0 - ratio * ratio) ** 2 * in_use
    kinds = jnp.arange(center_embed.shape[1])[:, None]
    species_hot = (kinds == own_species[None]).astype(jnp.float32)
    centre_hot = matmul_t(species_hot, member)
    other_hot = (kinds == other_species[None]).astype(jnp.float32)
    latent = envelope[None] * jax.nn.silu(
        matmul(radial_weight, basis)
        + matmul(center_embed, centre_hot)
        + matmul(neighbour_embed, other_hot)
    )
    channels = vector_weight.shape[0]
    vectors = envelope[None, None] * matmul(vector_weight, basis)[None] * unit[:, None, :]
    n_layers = env_weight.shape[0]
    for layer in range(n_layers):
        env_pairs = matmul(env_weight[layer], latent)
        spread = (unit[:, None, :] * env_pairs[None]).reshape(3 * channels, pair_count)
        environment = ENV_SCALE * matmul(spread, member)
        at_pairs = matmul_t(environment, member)
        at_pairs = at_pairs.reshape(3, channels, pair_count)
        scalars = jnp.sum(vectors * at_pairs, axis=0)
        update = matmul(latent_weight[layer], jnp.concatenate([latent, scalars], axis=0))
        if layer + 1 < n_layers:
            vectors = vectors + at_pairs * matmul(vector_gate, latent)[None]
        latent = latent + envelope[None] * jax.nn.silu(update)
    return jnp.sum(matmul(energy_weight[None], latent))


def per_device(
    positions,
    velocities,
    species,
    pair_table,
    live_blocks,
    owners,
    radial_weight,
    center_embed,
    neighbour_embed,
    vector_weight,
    env_weight,
    vector_gate,
    latent_weight,
    energy_weight,
):
    atoms_here = positions.shape[4]
    depth = atoms_here // 64
    zcount = lax.axis_size("gz")
    blocks_count = atoms_here // 128
    own_owners = owners[0, 0, 0]
    beside_xy = extended_2(positions, (("gx", 0), ("gy", 1)), 1)
    owner_row = jnp.repeat(own_owners.astype(jnp.float32), 128)
    owner_rows = jnp.broadcast_to(owner_row, beside_xy.shape[:3] + (1, atoms_here))
    carried = jnp.concatenate([beside_xy, owner_rows], axis=3)
    beside_all = extended_2(carried, (("gz", 2),), 1)
    extended = beside_all[:, :, :, :3].reshape(27, 3, atoms_here)
    beside_owners = beside_all[1, 1, :, 3]
    own_species = species[0, 0, 0]
    grad = jax.grad(pair_energy)(
        extended,
        pair_table[0, 0, 0],
        live_blocks[0, 0, 0],
        own_species,
        radial_weight,
        center_embed,
        neighbour_embed,
        vector_weight,
        env_weight,
        vector_gate,
        latent_weight,
        energy_weight,
    )
    grad = grad.reshape(3, 3, 3, 3, atoms_here)
    partial = fold_halo(grad, ("gx", "gy"))
    myself = lax.axis_index("gz")
    receivers = jnp.arange(zcount)
    sources = jnp.arange(zcount)
    beside_hits = (
        beside_owners.reshape(3, blocks_count, 128)[:, :, 0, None] == receivers.astype(jnp.float32)
    ).astype(jnp.float32)
    partial_blocks = partial.reshape(3, 3, blocks_count, 128).transpose(0, 2, 1, 3)
    per_receiver = jnp.sum(beside_hits[:, :, :, None, None] * partial_blocks[:, :, None], axis=1)
    source_of = (sources[None] == (myself + jnp.arange(3)[:, None] - 1) % zcount).astype(jnp.float32)
    grad_out = jnp.sum(source_of[:, None, :, None, None] * per_receiver[:, :, None], axis=0)
    inverse_mass = 1.0 / (1.0 + own_species.astype(jnp.float32))
    own_rows = jnp.concatenate(
        [positions[0, 0, 0], velocities[0, 0, 0], inverse_mass[None], jnp.ones((1, atoms_here), jnp.float32)],
        axis=0,
    )
    own_blocks = own_rows.reshape(8, blocks_count, 128).transpose(1, 0, 2)
    hits = (own_owners[:, None] == receivers[None]).astype(jnp.float32)
    own_out = jnp.sum(hits[:, :, None, None] * own_blocks[:, None], axis=0)
    at_self = (sources == myself).astype(jnp.float32)
    own_out = at_self[None, :, None, None] * own_out[:, None]
    outgoing = jnp.concatenate([grad_out, own_out], axis=2)
    arrived = lax.all_to_all(outgoing, "gz", split_axis=0, concat_axis=0, tiled=True)
    gathered = jnp.sum(arrived, axis=0)
    forces = -gathered[:, 0:3]
    old_pos = gathered[:, 3:6]
    old_vel = gathered[:, 6:9]
    arrived_mass = gathered[:, 9:10]
    flags = gathered[:, 10, 0]
    new_vel = old_vel + TIME_STEP * forces * arrived_mass
    new_pos = old_pos + TIME_STEP * new_vel
    state = jnp.concatenate([new_pos, new_vel, forces], axis=1)
    rise = flags * (sources - myself).astype(jnp.float32) * float(depth)
    arrived = state.at[:, 2, :].add(rise[:, None])
    return arrived[None, None, None]


def solution(mesh):
    in_specs = (
        P("gx", "gy", "gz", None, None),
        P("gx", "gy", "gz", None, None),
        P("gx", "gy", "gz", None),
        P("gx", "gy", "gz", None, None),
        P("gx", "gy", "gz"),
        P("gx", "gy", "gz", None),
        P(),
        P(),
        P(),
        P(),
        P(),
        P(),
        P(),
        P(),
    )
    out_specs = P("gx", "gy", "gz", None, None, None)
    return jax.shard_map(
        per_device, mesh=mesh, in_specs=in_specs, out_specs=out_specs, check_vma=False
    )
```

```python
import jax
import jax.numpy as jnp
from jax import lax
from jax.sharding import PartitionSpec as P


CUTOFF = 5.0
ENV_SCALE = 0.4
TIME_STEP = 0.2


def ring_pairs(axis):
    count = lax.axis_size(axis)
    forward = [(i, (i + 1) % count) for i in range(count)]
    backward = [(target, source) for source, target in forward]
    return forward, backward


def extended_2(block, sides, width):
    for axis, dim in sides:
        forward, backward = ring_pairs(axis)
        low = lax.ppermute(
            lax.slice_in_dim(block, block.shape[dim] - width, None, axis=dim), axis, forward
        )
        high = lax.ppermute(lax.slice_in_dim(block, 0, width, axis=dim), axis, backward)
        block = jnp.concatenate([low, block, high], axis=dim)
    return block


def fold_halo(grad, axes):
    for axis in axes:
        forward, backward = ring_pairs(axis)
        from_low = lax.ppermute(grad[2], axis, forward)
        from_high = lax.ppermute(grad[0], axis, backward)
        grad = grad[1] + from_low + from_high
    return grad


def matmul(left, right, precision=lax.Precision.HIGH):
    return jnp.dot(left, right, precision=precision)


def matmul_t(left, right, precision=lax.Precision.HIGH):
    return lax.dot_general(left, right, (((1,), (1,)), ((), ())), precision=precision)


def pair_energy(
    extended,
    pair_rows,
    live_count,
    own_species,
    radial_weight,
    center_embed,
    neighbour_embed,
    vector_weight,
    env_weight,
    vector_gate,
    latent_weight,
    energy_weight,
):
    slots, _, atoms_here = extended.shape
    pair_count = pair_rows.shape[1]
    depth = atoms_here // 64
    centres = pair_rows[0]
    neighbour = pair_rows[1]
    other_species = pair_rows[2]
    slot_index = neighbour // atoms_here
    atom_index = neighbour - slot_index * atoms_here
    offset_x = (slot_index // 9 - 1).astype(jnp.float32) * 8.0
    offset_y = (slot_index // 3 % 3 - 1).astype(jnp.float32) * 8.0
    offset_z = (slot_index % 3 - 1).astype(jnp.float32) * float(depth)
    shifts = jnp.stack([offset_x, offset_y, offset_z])
    atoms = jnp.arange(atoms_here)
    atom_hot = (atoms[:, None] == atom_index[None]).astype(jnp.float32)
    slot_hot = (jnp.arange(slots)[:, None] == slot_index[None]).astype(jnp.float32)
    member = (centres[:, None] == atoms[None]).astype(jnp.float32)
    by_atom = matmul(
        extended.reshape(slots * 3, atoms_here), atom_hot, lax.Precision.HIGHEST
    )
    far_end = jnp.sum(by_atom.reshape(slots, 3, pair_count) * slot_hot[:, None, :], axis=0)
    near_end = matmul_t(extended[13], member, lax.Precision.HIGHEST)
    displace = far_end + shifts - near_end
    distance = jnp.sqrt(jnp.sum(displace * displace, axis=0))
    unit = displace / distance
    orders = jnp.arange(1, radial_weight.shape[1] + 1).astype(jnp.float32)
    basis = (
        jnp.sqrt(2.0 / CUTOFF)
        * jnp.sin(orders[:, None] * jnp.pi * distance[None] / CUTOFF)
        / distance[None]
    )
    ratio = distance / CUTOFF
    in_use = (jnp.arange(pair_count) < live_count * 128).astype(jnp.float32)
    envelope = (1.0 - ratio * ratio) ** 2 * in_use
    kinds = jnp.arange(center_embed.shape[1])[:, None]
    species_hot = (kinds == own_species[None]).astype(jnp.float32)
    centre_hot = matmul_t(species_hot, member)
    other_hot = (kinds == other_species[None]).astype(jnp.float32)
    latent = envelope[None] * jax.nn.silu(
        matmul(radial_weight, basis)
        + matmul(center_embed, centre_hot)
        + matmul(neighbour_embed, other_hot)
    )
    channels = vector_weight.shape[0]
    vectors = envelope[None, None] * matmul(vector_weight, basis)[None] * unit[:, None, :]
    n_layers = env_weight.shape[0]
    for layer in range(n_layers):
        env_pairs = matmul(env_weight[layer], latent)
        spread = (unit[:, None, :] * env_pairs[None]).reshape(3 * channels, pair_count)
        environment = ENV_SCALE * matmul(spread, member)
        at_pairs = matmul_t(environment, member)
        at_pairs = at_pairs.reshape(3, channels, pair_count)
        scalars = jnp.sum(vectors * at_pairs, axis=0)
        update = matmul(latent_weight[layer], jnp.concatenate([latent, scalars], axis=0))
        if layer + 1 < n_layers:
            vectors = vectors + at_pairs * matmul(vector_gate, latent)[None]
        latent = latent + envelope[None] * jax.nn.silu(update)
    return jnp.sum(matmul(energy_weight[None], latent))


def per_device(
    positions,
    velocities,
    species,
    pair_table,
    live_blocks,
    owners,
    radial_weight,
    center_embed,
    neighbour_embed,
    vector_weight,
    env_weight,
    vector_gate,
    latent_weight,
    energy_weight,
):
    atoms_here = positions.shape[4]
    depth = atoms_here // 64
    zcount = lax.axis_size("gz")
    blocks_count = atoms_here // 128
    own_owners = owners[0, 0, 0]
    beside_xy = extended_2(positions, (("gx", 0), ("gy", 1)), 1)
    owner_row = jnp.repeat(own_owners.astype(jnp.float32), 128)
    owner_rows = jnp.broadcast_to(owner_row, beside_xy.shape[:3] + (1, atoms_here))
    carried = jnp.concatenate([beside_xy, owner_rows], axis=3)
    beside_all = extended_2(carried, (("gz", 2),), 1)
    extended = beside_all[:, :, :, :3].reshape(27, 3, atoms_here)
    beside_owners = beside_all[1, 1, :, 3]
    own_species = species[0, 0, 0]
    grad = jax.grad(pair_energy)(
        extended,
        pair_table[0, 0, 0],
        live_blocks[0, 0, 0],
        own_species,
        radial_weight,
        center_embed,
        neighbour_embed,
        vector_weight,
        env_weight,
        vector_gate,
        latent_weight,
        energy_weight,
    )
    grad = grad.reshape(3, 3, 3, 3, atoms_here)
    partial = fold_halo(grad, ("gx", "gy"))
    myself = lax.axis_index("gz")
    receivers = jnp.arange(zcount)
    sources = jnp.arange(zcount)
    beside_hits = (
        beside_owners.reshape(3, blocks_count, 128)[:, :, 0, None] == receivers.astype(jnp.float32)
    ).astype(jnp.float32)
    partial_blocks = partial.reshape(3, 3, blocks_count, 128).transpose(0, 2, 1, 3)
    per_receiver = jnp.sum(beside_hits[:, :, :, None, None] * partial_blocks[:, :, None], axis=1)
    source_of = (sources[None] == (myself + jnp.arange(3)[:, None] - 1) % zcount).astype(jnp.float32)
    grad_out = jnp.sum(source_of[:, None, :, None, None] * per_receiver[:, :, None], axis=0)
    inverse_mass = 1.0 / (1.0 + own_species.astype(jnp.float32))
    own_rows = jnp.concatenate(
        [positions[0, 0, 0], velocities[0, 0, 0], inverse_mass[None], jnp.ones((1, atoms_here), jnp.float32)],
        axis=0,
    )
    own_blocks = own_rows.reshape(8, blocks_count, 128).transpose(1, 0, 2)
    hits = (own_owners[:, None] == receivers[None]).astype(jnp.float32)
    own_out = jnp.sum(hits[:, :, None, None] * own_blocks[:, None], axis=0)
    outgoing = jnp.concatenate(
        [grad_out.reshape(zcount, zcount * 3, 128), own_out], axis=1
    )
    arrived = lax.all_to_all(outgoing, "gz", split_axis=0, concat_axis=0, tiled=True)
    grad_in = jnp.sum(arrived[:, : zcount * 3], axis=0).reshape(zcount, 3, 128)
    own_in = arrived[:, zcount * 3 :]
    forces = -grad_in
    old_pos = own_in[:, 0:3]
    old_vel = own_in[:, 3:6]
    arrived_mass = own_in[:, 6:7]
    flags = own_in[:, 7, 0]
    new_vel = old_vel + TIME_STEP * forces * arrived_mass
    new_pos = old_pos + TIME_STEP * new_vel
    state = jnp.concatenate([new_pos, new_vel, forces], axis=1)
    rise = flags * (sources - myself).astype(jnp.float32) * float(depth)
    arrived = state.at[:, 2, :].add(rise[:, None])
    return arrived[None, None, None]


def solution(mesh):
    in_specs = (
        P("gx", "gy", "gz", None, None),
        P("gx", "gy", "gz", None, None),
        P("gx", "gy", "gz", None),
        P("gx", "gy", "gz", None, None),
        P("gx", "gy", "gz"),
        P("gx", "gy", "gz", None),
        P(),
        P(),
        P(),
        P(),
        P(),
        P(),
        P(),
        P(),
    )
    out_specs = P("gx", "gy", "gz", None, None, None)

    return jax.shard_map(
        per_device, mesh=mesh, in_specs=in_specs, out_specs=out_specs, check_vma=False
    )
```

```python
import jax
import jax.numpy as jnp
from jax import lax
from jax.sharding import PartitionSpec as P


CUTOFF = 5.0
ENV_SCALE = 0.4
TIME_STEP = 0.2


def ring_pairs(axis):
    count = lax.axis_size(axis)
    forward = [(i, (i + 1) % count) for i in range(count)]
    backward = [(target, source) for source, target in forward]
    return forward, backward


def extended_2(block, sides, width):
    for axis, dim in sides:
        forward, backward = ring_pairs(axis)
        low = lax.ppermute(
            lax.slice_in_dim(block, block.shape[dim] - width, None, axis=dim), axis, forward
        )
        high = lax.ppermute(lax.slice_in_dim(block, 0, width, axis=dim), axis, backward)
        block = jnp.concatenate([low, block, high], axis=dim)
    return block


def fold_halo(grad, axes):
    for axis in axes:
        forward, backward = ring_pairs(axis)
        from_low = lax.ppermute(grad[2], axis, forward)
        from_high = lax.ppermute(grad[0], axis, backward)
        grad = grad[1] + from_low + from_high
    return grad


def matmul(left, right, precision=lax.Precision.HIGH):
    return jnp.dot(left, right, precision=precision)


def matmul_t(left, right, precision=lax.Precision.HIGH):
    return lax.dot_general(left, right, (((1,), (1,)), ((), ())), precision=precision)


def two_pass(left, right_bf16, dims):
    high = left.astype(jnp.bfloat16)
    low = (left - high.astype(jnp.float32)).astype(jnp.bfloat16)
    first = lax.dot_general(high, right_bf16, dims, preferred_element_type=jnp.float32)
    second = lax.dot_general(low, right_bf16, dims, preferred_element_type=jnp.float32)
    return first + second


PLAIN = (((1,), (0,)), ((), ()))
TRANSPOSED = (((1,), (1,)), ((), ()))


@jax.custom_vjp
def sum_by_centre(spread, member_bf16):
    return two_pass(spread, member_bf16, PLAIN)


def sum_by_centre_fwd(spread, member_bf16):
    return sum_by_centre(spread, member_bf16), member_bf16


def sum_by_centre_bwd(member_bf16, cotangent):
    return two_pass(cotangent, member_bf16, TRANSPOSED), None


sum_by_centre.defvjp(sum_by_centre_fwd, sum_by_centre_bwd)


@jax.custom_vjp
def spread_to_pairs(environment, member_bf16):
    return two_pass(environment, member_bf16, TRANSPOSED)


def spread_to_pairs_fwd(environment, member_bf16):
    return spread_to_pairs(environment, member_bf16), member_bf16


def spread_to_pairs_bwd(member_bf16, cotangent):
    return two_pass(cotangent, member_bf16, PLAIN), None


spread_to_pairs.defvjp(spread_to_pairs_fwd, spread_to_pairs_bwd)


def pair_energy(
    extended,
    pair_rows,
    live_count,
    own_species,
    radial_weight,
    center_embed,
    neighbour_embed,
    vector_weight,
    env_weight,
    vector_gate,
    latent_weight,
    energy_weight,
):
    slots, _, atoms_here = extended.shape
    pair_count = pair_rows.shape[1]
    depth = atoms_here // 64
    centres = pair_rows[0]
    neighbour = pair_rows[1]
    other_species = pair_rows[2]
    slot_index = neighbour // atoms_here
    atom_index = neighbour - slot_index * atoms_here
    offset_x = (slot_index // 9 - 1).astype(jnp.float32) * 8.0
    offset_y = (slot_index // 3 % 3 - 1).astype(jnp.float32) * 8.0
    offset_z = (slot_index % 3 - 1).astype(jnp.float32) * float(depth)
    shifts = jnp.stack([offset_x, offset_y, offset_z])
    atoms = jnp.arange(atoms_here)
    atom_hot = (atoms[:, None] == atom_index[None]).astype(jnp.float32)
    slot_hot = (jnp.arange(slots)[:, None] == slot_index[None]).astype(jnp.float32)
    member = (centres[:, None] == atoms[None]).astype(jnp.float32)
    by_atom = matmul(
        extended.reshape(slots * 3, atoms_here), atom_hot, lax.Precision.HIGHEST
    )
    far_end = jnp.sum(by_atom.reshape(slots, 3, pair_count) * slot_hot[:, None, :], axis=0)
    near_end = matmul_t(extended[13], member, lax.Precision.HIGHEST)
    displace = far_end + shifts - near_end
    distance = jnp.sqrt(jnp.sum(displace * displace, axis=0))
    unit = displace / distance
    orders = jnp.arange(1, radial_weight.shape[1] + 1).astype(jnp.float32)
    basis = (
        jnp.sqrt(2.0 / CUTOFF)
        * jnp.sin(orders[:, None] * jnp.pi * distance[None] / CUTOFF)
        / distance[None]
    )
    ratio = distance / CUTOFF
    in_use = (jnp.arange(pair_count) < live_count * 128).astype(jnp.float32)
    envelope = (1.0 - ratio * ratio) ** 2 * in_use
    kinds = jnp.arange(center_embed.shape[1])[:, None]
    species_hot = (kinds == own_species[None]).astype(jnp.float32)
    centre_hot = matmul_t(species_hot, member)
    other_hot = (kinds == other_species[None]).astype(jnp.float32)
    latent = envelope[None] * jax.nn.silu(
        matmul(radial_weight, basis)
        + matmul(center_embed, centre_hot)
        + matmul(neighbour_embed, other_hot)
    )
    channels = vector_weight.shape[0]
    vectors = envelope[None, None] * matmul(vector_weight, basis)[None] * unit[:, None, :]
    n_layers = env_weight.shape[0]
    member_bf16 = member.astype(jnp.bfloat16)
    for layer in range(n_layers):
        env_pairs = matmul(env_weight[layer], latent)
        spread = (unit[:, None, :] * env_pairs[None]).reshape(3 * channels, pair_count)
        environment = ENV_SCALE * sum_by_centre(spread, member_bf16)
        at_pairs = spread_to_pairs(environment, member_bf16)
        at_pairs = at_pairs.reshape(3, channels, pair_count)
        scalars = jnp.sum(vectors * at_pairs, axis=0)
        update = matmul(latent_weight[layer], jnp.concatenate([latent, scalars], axis=0))
        if layer + 1 < n_layers:
            vectors = vectors + at_pairs * matmul(vector_gate, latent)[None]
        latent = latent + envelope[None] * jax.nn.silu(update)
    return jnp.sum(matmul(energy_weight[None], latent))


def per_device(
    positions,
    velocities,
    species,
    pair_table,
    live_blocks,
    owners,
    radial_weight,
    center_embed,
    neighbour_embed,
    vector_weight,
    env_weight,
    vector_gate,
    latent_weight,
    energy_weight,
):
    atoms_here = positions.shape[4]
    depth = atoms_here // 64
    zcount = lax.axis_size("gz")
    blocks_count = atoms_here // 128
    own_owners = owners[0, 0, 0]
    beside_xy = extended_2(positions, (("gx", 0), ("gy", 1)), 1)
    owner_row = jnp.repeat(own_owners.astype(jnp.float32), 128)
    owner_rows = jnp.broadcast_to(owner_row, beside_xy.shape[:3] + (1, atoms_here))
    carried = jnp.concatenate([beside_xy, owner_rows], axis=3)
    beside_all = extended_2(carried, (("gz", 2),), 1)
    extended = beside_all[:, :, :, :3].reshape(27, 3, atoms_here)
    beside_owners = beside_all[1, 1, :, 3]
    own_species = species[0, 0, 0]
    grad = jax.grad(pair_energy)(
        extended,
        pair_table[0, 0, 0],
        live_blocks[0, 0, 0],
        own_species,
        radial_weight,
        center_embed,
        neighbour_embed,
        vector_weight,
        env_weight,
        vector_gate,
        latent_weight,
        energy_weight,
    )
    grad = grad.reshape(3, 3, 3, 3, atoms_here)
    partial = fold_halo(grad, ("gx", "gy"))
    myself = lax.axis_index("gz")
    receivers = jnp.arange(zcount)
    sources = jnp.arange(zcount)
    beside_hits = (
        beside_owners.reshape(3, blocks_count, 128)[:, :, 0, None] == receivers.astype(jnp.float32)
    ).astype(jnp.float32)
    partial_blocks = partial.reshape(3, 3, blocks_count, 128).transpose(0, 2, 1, 3)
    per_receiver = jnp.sum(beside_hits[:, :, :, None, None] * partial_blocks[:, :, None], axis=1)
    source_of = (sources[None] == (myself + jnp.arange(3)[:, None] - 1) % zcount).astype(jnp.float32)
    grad_out = jnp.sum(source_of[:, None, :, None, None] * per_receiver[:, :, None], axis=0)
    inverse_mass = 1.0 / (1.0 + own_species.astype(jnp.float32))
    own_rows = jnp.concatenate(
        [positions[0, 0, 0], velocities[0, 0, 0], inverse_mass[None], jnp.ones((1, atoms_here), jnp.float32)],
        axis=0,
    )
    own_blocks = own_rows.reshape(8, blocks_count, 128).transpose(1, 0, 2)
    hits = (own_owners[:, None] == receivers[None]).astype(jnp.float32)
    own_out = jnp.sum(hits[:, :, None, None] * own_blocks[:, None], axis=0)
    outgoing = jnp.concatenate(
        [grad_out.reshape(zcount, zcount * 3, 128), own_out], axis=1
    )
    arrived = lax.all_to_all(outgoing, "gz", split_axis=0, concat_axis=0, tiled=True)
    grad_in = jnp.sum(arrived[:, : zcount * 3], axis=0).reshape(zcount, 3, 128)
    own_in = arrived[:, zcount * 3 :]
    forces = -grad_in
    old_pos = own_in[:, 0:3]
    old_vel = own_in[:, 3:6]
    arrived_mass = own_in[:, 6:7]
    flags = own_in[:, 7, 0]
    new_vel = old_vel + TIME_STEP * forces * arrived_mass
    new_pos = old_pos + TIME_STEP * new_vel
    state = jnp.concatenate([new_pos, new_vel, forces], axis=1)
    rise = flags * (sources - myself).astype(jnp.float32) * float(depth)
    arrived = state.at[:, 2, :].add(rise[:, None])
    return arrived[None, None, None]


def solution(mesh):
    in_specs = (
        P("gx", "gy", "gz", None, None),
        P("gx", "gy", "gz", None, None),
        P("gx", "gy", "gz", None),
        P("gx", "gy", "gz", None, None),
        P("gx", "gy", "gz"),
        P("gx", "gy", "gz", None),
        P(),
        P(),
        P(),
        P(),
        P(),
        P(),
        P(),
        P(),
    )
    out_specs = P("gx", "gy", "gz", None, None, None)

    return jax.shard_map(
        per_device, mesh=mesh, in_specs=in_specs, out_specs=out_specs, check_vma=False
    )
```

```python
import jax
import jax.numpy as jnp
from jax import lax
from jax.sharding import PartitionSpec as P


CUTOFF = 5.0
ENV_SCALE = 0.4
TIME_STEP = 0.2


def ring_pairs(axis):
    count = lax.axis_size(axis)
    forward = [(i, (i + 1) % count) for i in range(count)]
    backward = [(target, source) for source, target in forward]
    return forward, backward


def extended_2(block, sides, width):
    for axis, dim in sides:
        forward, backward = ring_pairs(axis)
        low = lax.ppermute(
            lax.slice_in_dim(block, block.shape[dim] - width, None, axis=dim), axis, forward
        )
        high = lax.ppermute(lax.slice_in_dim(block, 0, width, axis=dim), axis, backward)
        block = jnp.concatenate([low, block, high], axis=dim)
    return block


def fold_halo(grad, axes):
    for axis in axes:
        forward, backward = ring_pairs(axis)
        from_low = lax.ppermute(grad[2], axis, forward)
        from_high = lax.ppermute(grad[0], axis, backward)
        grad = grad[1] + from_low + from_high
    return grad


def matmul(left, right, precision=lax.Precision.HIGH):
    return jnp.dot(left, right, precision=precision)


def matmul_t(left, right, precision=lax.Precision.HIGH):
    return lax.dot_general(left, right, (((1,), (1,)), ((), ())), precision=precision)


@jax.custom_vjp
def lookup(table, hot):
    return matmul(table, hot, lax.Precision.HIGHEST)


def lookup_fwd(table, hot):
    return lookup(table, hot), hot


def lookup_bwd(hot, cotangent):
    return matmul_t(cotangent, hot), None


lookup.defvjp(lookup_fwd, lookup_bwd)


@jax.custom_vjp
def lookup_t(table, hot):
    return matmul_t(table, hot, lax.Precision.HIGHEST)


def lookup_t_fwd(table, hot):
    return lookup_t(table, hot), hot


def lookup_t_bwd(hot, cotangent):
    return matmul(cotangent, hot), None


lookup_t.defvjp(lookup_t_fwd, lookup_t_bwd)


def pair_energy(
    extended,
    pair_rows,
    live_count,
    own_species,
    radial_weight,
    center_embed,
    neighbour_embed,
    vector_weight,
    env_weight,
    vector_gate,
    latent_weight,
    energy_weight,
):
    slots, _, atoms_here = extended.shape
    pair_count = pair_rows.shape[1]
    depth = atoms_here // 64
    centres = pair_rows[0]
    neighbour = pair_rows[1]
    other_species = pair_rows[2]
    slot_index = neighbour // atoms_here
    atom_index = neighbour - slot_index * atoms_here
    offset_x = (slot_index // 9 - 1).astype(jnp.float32) * 8.0
    offset_y = (slot_index // 3 % 3 - 1).astype(jnp.float32) * 8.0
    offset_z = (slot_index % 3 - 1).astype(jnp.float32) * float(depth)
    shifts = jnp.stack([offset_x, offset_y, offset_z])
    atoms = jnp.arange(atoms_here)
    atom_hot = (atoms[:, None] == atom_index[None]).astype(jnp.float32)
    slot_hot = (jnp.arange(slots)[:, None] == slot_index[None]).astype(jnp.float32)
    member = (centres[:, None] == atoms[None]).astype(jnp.float32)
    by_atom = lookup(extended.reshape(slots * 3, atoms_here), atom_hot)
    far_end = jnp.sum(by_atom.reshape(slots, 3, pair_count) * slot_hot[:, None, :], axis=0)
    near_end = lookup_t(extended[13], member)
    displace = far_end + shifts - near_end
    distance = jnp.sqrt(jnp.sum(displace * displace, axis=0))
    unit = displace / distance
    orders = jnp.arange(1, radial_weight.shape[1] + 1).astype(jnp.float32)
    basis = (
        jnp.sqrt(2.0 / CUTOFF)
        * jnp.sin(orders[:, None] * jnp.pi * distance[None] / CUTOFF)
        / distance[None]
    )
    ratio = distance / CUTOFF
    in_use = (jnp.arange(pair_count) < live_count * 128).astype(jnp.float32)
    envelope = (1.0 - ratio * ratio) ** 2 * in_use
    kinds = jnp.arange(center_embed.shape[1])[:, None]
    species_hot = (kinds == own_species[None]).astype(jnp.float32)
    centre_hot = matmul_t(species_hot, member)
    other_hot = (kinds == other_species[None]).astype(jnp.float32)
    latent = envelope[None] * jax.nn.silu(
        matmul(radial_weight, basis)
        + matmul(center_embed, centre_hot)
        + matmul(neighbour_embed, other_hot)
    )
    channels = vector_weight.shape[0]
    vectors = envelope[None, None] * matmul(vector_weight, basis)[None] * unit[:, None, :]
    n_layers = env_weight.shape[0]
    for layer in range(n_layers):
        env_pairs = matmul(env_weight[layer], latent)
        spread = (unit[:, None, :] * env_pairs[None]).reshape(3 * channels, pair_count)
        environment = ENV_SCALE * matmul(spread, member)
        at_pairs = matmul_t(environment, member)
        at_pairs = at_pairs.reshape(3, channels, pair_count)
        scalars = jnp.sum(vectors * at_pairs, axis=0)
        update = matmul(latent_weight[layer], jnp.concatenate([latent, scalars], axis=0))
        if layer + 1 < n_layers:
            vectors = vectors + at_pairs * matmul(vector_gate, latent)[None]
        latent = latent + envelope[None] * jax.nn.silu(update)
    return jnp.sum(matmul(energy_weight[None], latent))


def per_device(
    positions,
    velocities,
    species,
    pair_table,
    live_blocks,
    owners,
    radial_weight,
    center_embed,
    neighbour_embed,
    vector_weight,
    env_weight,
    vector_gate,
    latent_weight,
    energy_weight,
):
    atoms_here = positions.shape[4]
    depth = atoms_here // 64
    zcount = lax.axis_size("gz")
    blocks_count = atoms_here // 128
    own_owners = owners[0, 0, 0]
    beside_xy = extended_2(positions, (("gx", 0), ("gy", 1)), 1)
    owner_row = jnp.repeat(own_owners.astype(jnp.float32), 128)
    owner_rows = jnp.broadcast_to(owner_row, beside_xy.shape[:3] + (1, atoms_here))
    carried = jnp.concatenate([beside_xy, owner_rows], axis=3)
    beside_all = extended_2(carried, (("gz", 2),), 1)
    extended = beside_all[:, :, :, :3].reshape(27, 3, atoms_here)
    beside_owners = beside_all[1, 1, :, 3]
    own_species = species[0, 0, 0]
    grad = jax.grad(pair_energy)(
        extended,
        pair_table[0, 0, 0],
        live_blocks[0, 0, 0],
        own_species,
        radial_weight,
        center_embed,
        neighbour_embed,
        vector_weight,
        env_weight,
        vector_gate,
        latent_weight,
        energy_weight,
    )
    grad = grad.reshape(3, 3, 3, 3, atoms_here)
    partial = fold_halo(grad.transpose(1, 0, 2, 3, 4), ("gy", "gx"))
    myself = lax.axis_index("gz")
    receivers = jnp.arange(zcount)
    sources = jnp.arange(zcount)
    beside_hits = (
        beside_owners.reshape(3, blocks_count, 128)[:, :, 0, None] == receivers.astype(jnp.float32)
    ).astype(jnp.float32)
    partial_blocks = partial.reshape(3, 3, blocks_count, 128).transpose(0, 2, 1, 3)
    per_receiver = jnp.sum(beside_hits[:, :, :, None, None] * partial_blocks[:, :, None], axis=1)
    source_of = (sources[None] == (myself + jnp.arange(3)[:, None] - 1) % zcount).astype(jnp.float32)
    grad_out = jnp.sum(source_of[:, None, :, None, None] * per_receiver[:, :, None], axis=0)
    inverse_mass = 1.0 / (1.0 + own_species.astype(jnp.float32))
    own_rows = jnp.concatenate(
        [positions[0, 0, 0], velocities[0, 0, 0], inverse_mass[None], jnp.ones((1, atoms_here), jnp.float32)],
        axis=0,
    )
    own_blocks = own_rows.reshape(8, blocks_count, 128).transpose(1, 0, 2)
    hits = (own_owners[:, None] == receivers[None]).astype(jnp.float32)
    own_out = jnp.sum(hits[:, :, None, None] * own_blocks[:, None], axis=0)
    outgoing = jnp.concatenate(
        [grad_out.reshape(zcount, zcount * 3, 128), own_out], axis=1
    )
    arrived = lax.all_to_all(outgoing, "gz", split_axis=0, concat_axis=0, tiled=True)
    grad_in = jnp.sum(arrived[:, : zcount * 3], axis=0).reshape(zcount, 3, 128)
    own_in = arrived[:, zcount * 3 :]
    forces = -grad_in
    old_pos = own_in[:, 0:3]
    old_vel = own_in[:, 3:6]
    arrived_mass = own_in[:, 6:7]
    flags = own_in[:, 7, 0]
    new_vel = old_vel + TIME_STEP * forces * arrived_mass
    new_pos = old_pos + TIME_STEP * new_vel
    state = jnp.concatenate([new_pos, new_vel, forces], axis=1)
    rise = flags * (sources - myself).astype(jnp.float32) * float(depth)
    arrived = state.at[:, 2, :].add(rise[:, None])
    return arrived[None, None, None]


def solution(mesh):
    in_specs = (
        P("gx", "gy", "gz", None, None),
        P("gx", "gy", "gz", None, None),
        P("gx", "gy", "gz", None),
        P("gx", "gy", "gz", None, None),
        P("gx", "gy", "gz"),
        P("gx", "gy", "gz", None),
        P(),
        P(),
        P(),
        P(),
        P(),
        P(),
        P(),
        P(),
    )
    out_specs = P("gx", "gy", "gz", None, None, None)

    return jax.shard_map(
        per_device, mesh=mesh, in_specs=in_specs, out_specs=out_specs, check_vma=False
    )
```
